256 devices in a mesh: seq: 32 (over y, x, z_lo), tp: 8 (over z_hi, core).
Axes of the slice: x: 4, y: 4, z: 8 (z_hi: 4, z_lo: 2; z = z_hi * 2 + z_lo), core: 2. Of those that a mesh axis runs over, the one named last changes fastest.
Arguments:
- tokens: bfloat16 [32768, 2048], P('seq'), may hold values from -20 to 20
- w_query: bfloat16 [2048, 2048], P(None, 'tp'), may hold values from -0.15467961 to 0.15467961
- w_kv: bfloat16 [2048, 512], replicated, may hold values from -0.110485435 to 0.110485435
- w_out: bfloat16 [2048, 2048], P('tp'), may hold values from -6 to 6
- seg_start: int32 [32768], P('seq'), may hold values from 0 to 32752, as said below
- page_owner: int32 [2048], replicated, may hold values from 0 to 31, as said below
- page_slot: int32 [2048], replicated, may hold values from 0 to 127, as said below
Outputs:
- layer_out: bfloat16 [32768, 2048], P('seq', 'tp')
- kv_cache: bfloat16 [65536, 512], P('seq', 'tp')
The draws below stay inside these ranges and needn't reach their ends.
Inputs may be any that keep to these rules, and one draw needn't show every extreme that they name: seg_start[t] is the first position of the prompt that holds token t: it never falls along the stream, is a multiple of 16, is at most t, and equals t at each prompt's first token; the last page begins a prompt. `page_owner`: among the 64 pages of one stream block no owner is named more than 4 times; one owner is named exactly 4 times by the pages of every block. `page_slot`: pages with the same owner have distinct slots.
All inputs are finite; a program needn't handle non-finite values.
Results may differ from the reference program's by a relative error of at most 0.015.
Values may be sent and summed in bfloat16 or wider, within the bound.
No kernel may reach another device: no remote copies, remote signals or barrier semaphores. Data moves between devices by JAX's collectives and lax.ppermute only.
A program may use at most 64 MiB of HBM per device.

```python
import jax
import jax.numpy as jnp
from jax import lax

D = 2048
H = 32
KVH = 4
HD = 64
WINDOW = 2048
PAGE = 16
TOK_DEV = 1024
TOKENS = 32768
PAGES_DEV = 64
PAGES = 2048
CAP = 4
CACHE_PAGES = 128
CACHE_ROWS = 2048
N_SEQ = 32
N_TP = 8


def draw_tokens(key, part):
    base_key = jax.random.fold_in(key, 0)
    result = jnp.clip(jax.random.normal(base_key, (TOKENS, D), jnp.float32), -4.0, 4.0)
    return result.astype(jnp.bfloat16)


def projection_pair(key):
    first_key, second_key = jax.random.split(jax.random.fold_in(key, 7))
    kv_part = jnp.clip(jax.random.normal(first_key, (D, KVH, 2, HD), jnp.float32), -5.0, 5.0) * D ** (-0.5)
    own_part = jnp.clip(jax.random.normal(second_key, (D, KVH, H // KVH, HD), jnp.float32), -5.0, 5.0) * D ** (-0.5)
    query_part = own_part
    return (query_part.reshape(D, H * HD), kv_part.reshape(D, KVH * 2 * HD))


def draw_w_query(key, part):
    return projection_pair(key)[0].astype(jnp.bfloat16)


def draw_w_kv(key, part):
    return projection_pair(key)[1].astype(jnp.bfloat16)


def draw_seg_start(key, part):
    rate_key, flag_key = jax.random.split(jax.random.fold_in(key, 3))
    rate_table = jnp.array([2, 4, 16, 64], jnp.int32)
    rates = rate_table[jax.random.randint(rate_key, (N_SEQ,), 0, 4)]
    page_rates = jnp.repeat(rates, PAGES_DEV)
    flags = jax.random.randint(flag_key, (PAGES,), 0, 1 << 20) % page_rates == 0
    flags = flags.at[0].set(True)
    flags = flags.at[PAGES - 1].set(True)
    page_index = jnp.arange(PAGES, dtype=jnp.int32)
    start_page = lax.cummax(jnp.where(flags, page_index, 0), axis=0)
    return jnp.repeat(start_page * PAGE, PAGE).astype(jnp.int32)


def page_layout(key):
    base_key = jax.random.fold_in(key, 5)
    heavy = jax.random.randint(jax.random.fold_in(base_key, 1), (), 0, N_SEQ)
    block_keys = jax.random.split(jax.random.fold_in(base_key, 2), N_SEQ)

    def one_block(block_key):
        order_key, place_key, label_key = jax.random.split(block_key, 3)
        others = CAP + jax.random.permutation(order_key, N_SEQ * CAP - CAP)
        items = (jnp.concatenate([jnp.arange(CAP, dtype=jnp.int32), others.astype(jnp.int32)]) // CAP)[:PAGES_DEV]
        items = items[jax.random.permutation(place_key, PAGES_DEV)]
        relabel = jax.random.permutation(label_key, N_SEQ).astype(jnp.int32)
        where_heavy = jnp.argmax(relabel == heavy)
        relabel = relabel.at[where_heavy].set(relabel[0]).at[0].set(heavy)
        return relabel[items]
    owners = jax.vmap(one_block)(block_keys).reshape(PAGES).astype(jnp.int32)
    owner_hot = (owners[:, None] == jnp.arange(N_SEQ, dtype=jnp.int32)[None, :]).astype(jnp.int32)
    ranks = jnp.sum((jnp.cumsum(owner_hot, axis=0) - owner_hot) * owner_hot, axis=1)
    slot_keys = jax.random.split(jax.random.fold_in(base_key, 3), N_SEQ)
    slot_tables = jax.vmap(lambda slot_key: jax.random.permutation(slot_key, CACHE_PAGES))(slot_keys)
    slots = slot_tables[owners, ranks].astype(jnp.int32)
    return (owners, slots)


def draw_page_owner(key, part):
    return page_layout(key)[0]


def draw_page_slot(key, part):
    return page_layout(key)[1]


def with_spikes(values, stream_key, source, target, shards_of, factor):
    owner, partner = [(jnp.arange(values.shape[axis_at]) // (values.shape[axis_at] // shards_of)).reshape([-1 if axis == axis_at else 1 for axis in range(values.ndim)]) for axis_at in (source, target)]
    chosen = jax.random.permutation(stream_key, shards_of)[partner]
    strong = (owner == chosen) | (owner == (partner + shards_of // 2) % shards_of)
    return jnp.where(strong, factor * values, values)


def shard_levels(own_key, shape, pieces, low, top_value):
    level, own = 1.0, jax.random.fold_in(own_key, 6)
    for dim, parts in pieces:
        draws = jnp.exp(jax.random.uniform(jax.random.fold_in(own, dim), (parts,), jnp.float32, low / len(pieces), top_value / len(pieces)))
        level = level * jnp.repeat(draws, shape[dim] // parts).reshape([-1 if axis == dim else 1 for axis in range(len(shape))])
    return level


def gaussian_with(own_key, extent, width, limit, shards, heavy, held_as=jnp.bfloat16):
    drawn = width * jax.random.normal(own_key, extent, jnp.float32)
    if shards:
        drawn = drawn * shard_levels(own_key, extent, shards, -0.22, 0.18)
    return jnp.clip(with_spikes(drawn, jax.random.fold_in(own_key, 3), *heavy), -limit, limit).astype(held_as)


def setup_inputs(seed: int = 0) -> dict:
    splits = jax.random.split(jax.random.key(seed), 8)
    return {
        "tokens": draw_tokens(jax.random.fold_in(splits[7], 71), 0),
        "w_query": draw_w_query(jax.random.fold_in(splits[7], 71), 0),
        "w_kv": draw_w_kv(jax.random.fold_in(splits[7], 71), 0),
        "w_out": gaussian_with(splits[3], (H * HD, D), 0.3, 6.0, ((0, 8),), (0, 1, 8, 2.0)),
        "seg_start": draw_seg_start(jax.random.fold_in(splits[7], 71), 0),
        "page_owner": draw_page_owner(jax.random.fold_in(splits[7], 71), 0),
        "page_slot": draw_page_slot(jax.random.fold_in(splits[7], 71), 0),
    }


masked_value = -1.0e30


def attend_band(query_block, band_block, positions_q, positions_k, starts):
    keys_block = band_block[:, :, 0, :].astype(jnp.float32)
    values_block = band_block[:, :, 1, :].astype(jnp.float32)
    head_size = query_block.shape[-1]
    scores = jnp.einsum("qkgd,ckd->kgqc", query_block.astype(jnp.float32), keys_block) * (head_size ** -0.5)
    lower_bound = jnp.maximum(starts, positions_q - WINDOW + 1)
    visible = (positions_k[None, :] >= lower_bound[:, None]) & (positions_k[None, :] <= positions_q[:, None])
    scores = jnp.where(visible, scores, masked_value)
    largest = jnp.max(scores, axis=-1, keepdims=True)
    powered = jnp.exp(scores - largest)
    row_total = jnp.sum(powered, axis=-1, keepdims=True)
    weights = powered.astype(jnp.bfloat16)
    result = jnp.einsum("kgqc,ckd->kgqd", weights.astype(jnp.float32), values_block) / row_total
    return jnp.transpose(result, (2, 0, 1, 3)).astype(jnp.bfloat16)


def reference(tokens, w_query, w_kv, w_out, seg_start, page_owner, page_slot):
    group_size = H // KVH
    queries = jnp.dot(tokens, w_query, preferred_element_type=jnp.float32).astype(jnp.bfloat16)
    key_value = jnp.dot(tokens, w_kv, preferred_element_type=jnp.float32).astype(jnp.bfloat16)
    padded = jnp.concatenate([jnp.zeros((WINDOW, KVH * 2 * HD), key_value.dtype), key_value], axis=0)
    padded = padded.reshape(TOKENS + WINDOW, KVH, 2, HD)
    query_heads = queries.reshape(TOKENS, KVH, group_size, HD)
    block_rows = min(256, TOK_DEV)

    def one_block(block_idx):
        first_row = (block_idx * block_rows).astype(jnp.int32)
        query_block = lax.dynamic_slice_in_dim(query_heads, first_row, block_rows, 0)
        band_block = lax.dynamic_slice_in_dim(padded, first_row, WINDOW + block_rows, 0)
        starts = lax.dynamic_slice_in_dim(seg_start, first_row, block_rows, 0)
        positions_q = first_row + jnp.arange(block_rows, dtype=jnp.int32)
        positions_k = first_row - WINDOW + jnp.arange(WINDOW + block_rows, dtype=jnp.int32)
        return attend_band(query_block, band_block, positions_q, positions_k, starts)

    attended = lax.map(one_block, jnp.arange(TOKENS // block_rows, dtype=jnp.int32))
    attended = attended.reshape(TOKENS, H * HD)
    heads_cols = H * HD // N_TP
    summed = jnp.zeros((TOKENS, D), jnp.float32)
    for group_idx in range(N_TP):
        term = jnp.dot(attended[:, group_idx * heads_cols:(group_idx + 1) * heads_cols],
                       w_out[group_idx * heads_cols:(group_idx + 1) * heads_cols],
                       preferred_element_type=jnp.float32).astype(jnp.bfloat16)
        term = lax.optimization_barrier(term)
        summed = summed + term.astype(jnp.float32)
    layer_out = summed.astype(jnp.bfloat16)
    cache_pages = jnp.zeros((N_SEQ * CACHE_PAGES, PAGE, KVH * 2 * HD), key_value.dtype)
    target = (page_owner * CACHE_PAGES + page_slot).astype(jnp.int32)
    cache_pages = cache_pages.at[target].set(key_value.reshape(PAGES, PAGE, KVH * 2 * HD))
    kv_cache = cache_pages.reshape(N_SEQ * CACHE_ROWS, KVH * 2 * HD)
    return layer_out, kv_cache
```

```python
import jax
import jax.numpy as jnp
from jax import lax
from jax.sharding import PartitionSpec as P

H = 32
KVH = 4
HD = 64
WINDOW = 2048
PAGE = 16


masked_value = -1e30


def passed_along(value, axis, steps):
    count = lax.axis_size(axis)
    leading, last = (max(0, -steps), min(count, count - steps))
    return lax.ppermute(value, axis, [(source, source + steps) for source in range(leading, last)])


def attend_band(query_block, band_block, positions_q, positions_k, starts):
    keys_block = band_block[:, :, 0, :]
    values_block = band_block[:, :, 1, :]
    head_size = query_block.shape[-1]
    scores = jnp.einsum(
        "qkgd,ckd->kgqc", query_block, keys_block, preferred_element_type=jnp.float32
    ) * head_size ** (-0.5)
    lower_bound = jnp.maximum(starts, positions_q - WINDOW + 1)
    visible = (positions_k[None, :] >= lower_bound[:, None]) & (
        positions_k[None, :] <= positions_q[:, None]
    )
    scores = jnp.where(visible, scores, masked_value)
    largest = jnp.max(scores, axis=-1, keepdims=True)
    powered = jnp.exp(scores - largest)
    row_total = jnp.sum(powered, axis=-1, keepdims=True)
    weights = powered.astype(jnp.bfloat16)
    result = (
        jnp.einsum("kgqc,ckd->kgqd", weights, values_block, preferred_element_type=jnp.float32)
        / row_total
    )
    return jnp.transpose(result, (2, 0, 1, 3)).astype(jnp.bfloat16)


def body(tokens, w_query, w_kv, w_out, seg_start, page_owner, page_slot):
    seq_index = lax.axis_index("seq")
    tp_index = lax.axis_index("tp")
    seq_count = lax.axis_size("seq")
    tp_count = lax.axis_size("tp")
    tok_rows = tokens.shape[0]
    group_size = H // KVH
    heads_dev = H // tp_count
    kv_heads_dev = max(1, heads_dev // group_size)
    kv_width = kv_heads_dev * 2 * HD
    cache_width = KVH * 2 * HD // tp_count
    first_col = tp_index * heads_dev // group_size * 2 * HD
    queries = jnp.dot(tokens, w_query, preferred_element_type=jnp.float32).astype(jnp.bfloat16)
    w_local = lax.dynamic_slice_in_dim(w_kv, first_col, kv_width, 1)
    key_value = jnp.dot(tokens, w_local, preferred_element_type=jnp.float32).astype(jnp.bfloat16)
    own_cols = lax.dynamic_slice_in_dim(
        key_value, tp_index * cache_width - first_col, cache_width, 1
    )
    pages_dev = tok_rows // PAGE
    slots_per = max(2, 2 * pages_dev // seq_count)
    cache_slots = seq_count * slots_per
    owners_all = page_owner.reshape(seq_count, pages_dev)
    owner_hot = (
        owners_all[:, :, None] == jnp.arange(seq_count, dtype=jnp.int32)[None, None, :]
    ).astype(jnp.int32)
    local_rank = jnp.sum((jnp.cumsum(owner_hot, axis=1) - owner_hot) * owner_hot, axis=2)
    column_of = jnp.arange(seq_count, dtype=jnp.int32)[:, None] * slots_per + local_rank
    own_owner = lax.dynamic_index_in_dim(owners_all, seq_index, 0, keepdims=False)
    own_rank = lax.dynamic_index_in_dim(local_rank, seq_index, 0, keepdims=False)
    destination = own_owner * slots_per + own_rank
    send_table = (jnp.arange(cache_slots, dtype=jnp.int32)[:, None] == destination[None, :]).astype(
        jnp.bfloat16
    )
    page_rows = own_cols.reshape(pages_dev, PAGE * cache_width)
    outgoing_pages = jnp.dot(send_table, page_rows, preferred_element_type=jnp.float32).astype(
        jnp.bfloat16
    )
    outgoing_pages = outgoing_pages.reshape(seq_count, slots_per, PAGE * cache_width)
    arrived = lax.all_to_all(outgoing_pages, "seq", split_axis=0, concat_axis=0, tiled=True)
    owned_here = page_owner == seq_index
    place_table = (
        (page_slot[None, :] == jnp.arange(cache_slots, dtype=jnp.int32)[:, None])
        & owned_here[None, :]
    ).astype(jnp.bfloat16)
    pick_table = (
        column_of.reshape(-1)[:, None] == jnp.arange(cache_slots, dtype=jnp.int32)[None, :]
    ).astype(jnp.bfloat16)
    route_table = jnp.dot(place_table, pick_table, preferred_element_type=jnp.float32).astype(
        jnp.bfloat16
    )
    cache_local = jnp.dot(
        route_table,
        arrived.reshape(cache_slots, PAGE * cache_width),
        preferred_element_type=jnp.float32,
    )
    kv_cache = cache_local.astype(jnp.bfloat16).reshape(cache_slots * PAGE, cache_width)
    blocks_back = WINDOW // tok_rows
    pieces = []
    for distance in range(blocks_back, 0, -1):
        pieces.append(passed_along(key_value, "seq", distance))
    behind = jnp.concatenate(pieces, axis=0)
    band_all = jnp.concatenate([behind, key_value], axis=0).reshape(-1, kv_heads_dev, 2, HD)
    query_heads = queries.reshape(tok_rows, kv_heads_dev, heads_dev // kv_heads_dev, HD)
    block_rows = min(256, tok_rows)
    base_position = seq_index * tok_rows

    def one_block(block_idx):
        first_row = block_idx * block_rows
        query_block = lax.dynamic_slice_in_dim(query_heads, first_row, block_rows, 0)
        band_block = lax.dynamic_slice_in_dim(band_all, first_row, WINDOW + block_rows, 0)
        starts = lax.dynamic_slice_in_dim(seg_start, first_row, block_rows, 0)
        positions_q = base_position + first_row + jnp.arange(block_rows, dtype=jnp.int32)
        positions_k = (
            base_position + first_row - WINDOW + jnp.arange(WINDOW + block_rows, dtype=jnp.int32)
        )
        return attend_band(query_block, band_block, positions_q, positions_k, starts)

    out_blocks = []
    for block_idx in range(tok_rows // block_rows):
        attended = one_block(block_idx).reshape(block_rows, heads_dev * HD)
        projected = jnp.dot(attended, w_out, preferred_element_type=jnp.float32)
        out_blocks.append(
            lax.psum_scatter(projected.astype(jnp.bfloat16), "tp", scatter_dimension=1, tiled=True)
        )
    layer_out = jnp.concatenate(out_blocks, axis=0)
    return (layer_out, kv_cache)


def solution(mesh):
    return jax.shard_map(
        body,
        mesh=mesh,
        in_specs=(P("seq", None), P(None, "tp"), P(), P("tp", None), P("seq"), P(), P()),
        out_specs=(P("seq", "tp"), P("seq", "tp")),
        check_vma=False,
    )
```

```python
import jax
import jax.numpy as jnp
from jax import lax
from jax.sharding import PartitionSpec as P

H = 32
KVH = 4
HD = 64
WINDOW = 2048
PAGE = 16


masked_value = -1e30


def passed_along(value, axis, steps):
    count = lax.axis_size(axis)
    leading, last = (max(0, -steps), min(count, count - steps))
    return lax.ppermute(value, axis, [(source, source + steps) for source in range(leading, last)])


def attend_band(query_block, band_block, positions_q, positions_k, starts):
    keys_block = band_block[:, :, 0, :]
    values_block = band_block[:, :, 1, :]
    head_size = query_block.shape[-1]
    scores = jnp.einsum(
        "qkgd,ckd->kgqc", query_block, keys_block, preferred_element_type=jnp.float32
    ) * head_size ** (-0.5)
    lower_bound = jnp.maximum(starts, positions_q - WINDOW + 1)
    visible = (positions_k[None, :] >= lower_bound[:, None]) & (
        positions_k[None, :] <= positions_q[:, None]
    )
    scores = jnp.where(visible, scores, masked_value)
    largest = jnp.max(scores, axis=-1, keepdims=True)
    powered = jnp.exp(scores - largest)
    row_total = jnp.sum(powered, axis=-1, keepdims=True)
    weights = powered.astype(jnp.bfloat16)
    result = (
        jnp.einsum("kgqc,ckd->kgqd", weights, values_block, preferred_element_type=jnp.float32)
        / row_total
    )
    return jnp.transpose(result, (2, 0, 1, 3)).astype(jnp.bfloat16)


def body(tokens, w_query, w_kv, w_out, seg_start, page_owner, page_slot):
    seq_index = lax.axis_index("seq")
    tp_index = lax.axis_index("tp")
    seq_count = lax.axis_size("seq")
    tp_count = lax.axis_size("tp")
    tok_rows = tokens.shape[0]
    group_size = H // KVH
    heads_dev = H // tp_count
    kv_heads_dev = max(1, heads_dev // group_size)
    kv_width = kv_heads_dev * 2 * HD
    cache_width = KVH * 2 * HD // tp_count
    first_col = tp_index * heads_dev // group_size * 2 * HD
    queries = jnp.dot(tokens, w_query, preferred_element_type=jnp.float32).astype(jnp.bfloat16)
    w_local = lax.dynamic_slice_in_dim(w_kv, first_col, kv_width, 1)
    key_value = jnp.dot(tokens, w_local, preferred_element_type=jnp.float32).astype(jnp.bfloat16)
    own_cols = lax.dynamic_slice_in_dim(
        key_value, tp_index * cache_width - first_col, cache_width, 1
    )
    pages_dev = tok_rows // PAGE
    slots_per = max(2, 2 * pages_dev // seq_count)
    cache_slots = seq_count * slots_per
    owners_all = page_owner.reshape(seq_count, pages_dev)
    owner_hot = (
        owners_all[:, :, None] == jnp.arange(seq_count, dtype=jnp.int32)[None, None, :]
    ).astype(jnp.int32)
    local_rank = jnp.sum((jnp.cumsum(owner_hot, axis=1) - owner_hot) * owner_hot, axis=2)
    column_of = jnp.arange(seq_count, dtype=jnp.int32)[:, None] * slots_per + local_rank
    own_owner = lax.dynamic_index_in_dim(owners_all, seq_index, 0, keepdims=False)
    own_rank = lax.dynamic_index_in_dim(local_rank, seq_index, 0, keepdims=False)
    destination = own_owner * slots_per + own_rank
    send_table = (jnp.arange(cache_slots, dtype=jnp.int32)[:, None] == destination[None, :]).astype(
        jnp.bfloat16
    )
    page_rows = own_cols.reshape(pages_dev, PAGE * cache_width)
    outgoing_pages = jnp.dot(send_table, page_rows, preferred_element_type=jnp.float32).astype(
        jnp.bfloat16
    )
    outgoing_pages = outgoing_pages.reshape(seq_count, slots_per, PAGE * cache_width)
    arrived = lax.all_to_all(outgoing_pages, "seq", split_axis=0, concat_axis=0, tiled=True)
    owned_here = page_owner == seq_index
    place_table = (
        (page_slot[None, :] == jnp.arange(cache_slots, dtype=jnp.int32)[:, None])
        & owned_here[None, :]
    ).astype(jnp.bfloat16)
    pick_table = (
        column_of.reshape(-1)[:, None] == jnp.arange(cache_slots, dtype=jnp.int32)[None, :]
    ).astype(jnp.bfloat16)
    route_table = jnp.dot(place_table, pick_table, preferred_element_type=jnp.float32).astype(
        jnp.bfloat16
    )
    cache_local = jnp.dot(
        route_table,
        arrived.reshape(cache_slots, PAGE * cache_width),
        preferred_element_type=jnp.float32,
    )
    kv_cache = cache_local.astype(jnp.bfloat16).reshape(cache_slots * PAGE, cache_width)
    blocks_back = WINDOW // tok_rows
    pieces = []
    for distance in range(blocks_back, 0, -1):
        pieces.append(passed_along(key_value, "seq", distance))
    behind = jnp.concatenate(pieces, axis=0)
    band_all = jnp.concatenate([behind, key_value], axis=0).reshape(-1, kv_heads_dev, 2, HD)
    query_heads = queries.reshape(tok_rows, kv_heads_dev, heads_dev // kv_heads_dev, HD)
    block_rows = min(256, tok_rows)
    base_position = seq_index * tok_rows

    def one_block(block_idx, query_block):
        first_row = block_idx * block_rows
        band_block = lax.dynamic_slice_in_dim(band_all, first_row, WINDOW + block_rows, 0)
        starts = lax.dynamic_slice_in_dim(seg_start, first_row, block_rows, 0)
        positions_q = base_position + first_row + jnp.arange(block_rows, dtype=jnp.int32)
        positions_k = (
            base_position + first_row - WINDOW + jnp.arange(WINDOW + block_rows, dtype=jnp.int32)
        )
        return attend_band(query_block, band_block, positions_q, positions_k, starts)

    col_width = w_out.shape[1] // tp_count
    chips = tp_count // 2
    core = tp_index % 2
    chip = tp_index // 2
    swap_pairs = [(p, p ^ 1) for p in range(tp_count)]

    def reduce_in_chip(projected):
        rows = projected.shape[0]
        parts = projected.astype(jnp.bfloat16).reshape(rows, chips, 2, col_width)
        keep = lax.dynamic_index_in_dim(parts, core, 2, keepdims=False)
        send = lax.dynamic_index_in_dim(parts, 1 - core, 2, keepdims=False)
        got = lax.ppermute(send, "tp", swap_pairs)
        return (keep.astype(jnp.float32) + got.astype(jnp.float32)).astype(jnp.bfloat16)

    def reduce_across_chips(chip_sum):
        total = lax.dynamic_index_in_dim(chip_sum, chip, 1, keepdims=False).astype(jnp.float32)
        for shift in range(1, chips):
            piece = lax.dynamic_index_in_dim(chip_sum, (chip + shift) % chips, 1, keepdims=False)
            moved = lax.ppermute(
                piece, "tp", [(p, (p + 2 * shift) % tp_count) for p in range(tp_count)]
            )
            total = total + moved.astype(jnp.float32)
        return total.astype(jnp.bfloat16)

    out_blocks = []
    pending = None
    for block_idx in range(tok_rows // block_rows):
        query_block = query_heads[block_idx * block_rows:(block_idx + 1) * block_rows]
        if pending is not None:
            pending, query_block = lax.optimization_barrier((pending, query_block))
            out_blocks.append(reduce_across_chips(pending))
        attended = one_block(block_idx, query_block).reshape(block_rows, heads_dev * HD)
        projected = jnp.dot(attended, w_out, preferred_element_type=jnp.float32)
        pending = reduce_in_chip(projected)
    out_blocks.append(reduce_across_chips(pending))
    layer_out = jnp.concatenate(out_blocks, axis=0)
    return (layer_out, kv_cache)


def solution(mesh):
    return jax.shard_map(
        body,
        mesh=mesh,
        in_specs=(P("seq", None), P(None, "tp"), P(), P("tp", None), P("seq"), P(), P()),
        out_specs=(P("seq", "tp"), P("seq", "tp")),
        check_vma=False,
    )
```

```python
import jax
import jax.numpy as jnp
from jax import lax
from jax.sharding import PartitionSpec as P

H = 32
KVH = 4
HD = 64
WINDOW = 2048
PAGE = 16


masked_value = -1e30


def passed_along(value, axis, steps):
    count = lax.axis_size(axis)
    leading, last = (max(0, -steps), min(count, count - steps))
    return lax.ppermute(value, axis, [(source, source + steps) for source in range(leading, last)])


def attend_band(query_block, band_block, positions_q, positions_k, starts):
    keys_block = band_block[:, :, 0, :]
    values_block = band_block[:, :, 1, :]
    head_size = query_block.shape[-1]
    scores = jnp.einsum(
        "qkgd,ckd->kgqc", query_block, keys_block, preferred_element_type=jnp.float32
    ) * head_size ** (-0.5)
    lower_bound = jnp.maximum(starts, positions_q - WINDOW + 1)
    visible = (positions_k[None, :] >= lower_bound[:, None]) & (
        positions_k[None, :] <= positions_q[:, None]
    )
    scores = jnp.where(visible, scores, masked_value)
    largest = jnp.max(scores, axis=-1, keepdims=True)
    powered = jnp.exp(scores - largest)
    row_total = jnp.sum(powered, axis=-1, keepdims=True)
    weights = powered.astype(jnp.bfloat16)
    result = (
        jnp.einsum("kgqc,ckd->kgqd", weights, values_block, preferred_element_type=jnp.float32)
        / row_total
    )
    return jnp.transpose(result, (2, 0, 1, 3)).astype(jnp.bfloat16)


def body(tokens, w_query, w_kv, w_out, seg_start, page_owner, page_slot):
    seq_index = lax.axis_index("seq")
    tp_index = lax.axis_index("tp")
    seq_count = lax.axis_size("seq")
    tp_count = lax.axis_size("tp")
    tok_rows = tokens.shape[0]
    group_size = H // KVH
    heads_dev = H // tp_count
    kv_heads_dev = max(1, heads_dev // group_size)
    kv_width = kv_heads_dev * 2 * HD
    cache_width = KVH * 2 * HD // tp_count
    first_col = tp_index * heads_dev // group_size * 2 * HD
    queries = jnp.dot(tokens, w_query, preferred_element_type=jnp.float32).astype(jnp.bfloat16)
    w_local = lax.dynamic_slice_in_dim(w_kv, first_col, kv_width, 1)
    key_value = jnp.dot(tokens, w_local, preferred_element_type=jnp.float32).astype(jnp.bfloat16)
    own_cols = lax.dynamic_slice_in_dim(
        key_value, tp_index * cache_width - first_col, cache_width, 1
    )
    pages_dev = tok_rows // PAGE
    slots_per = max(2, 2 * pages_dev // seq_count)
    cache_slots = seq_count * slots_per
    owners_all = page_owner.reshape(seq_count, pages_dev)
    owner_hot = (
        owners_all[:, :, None] == jnp.arange(seq_count, dtype=jnp.int32)[None, None, :]
    ).astype(jnp.int32)
    local_rank = jnp.sum((jnp.cumsum(owner_hot, axis=1) - owner_hot) * owner_hot, axis=2)
    column_of = jnp.arange(seq_count, dtype=jnp.int32)[:, None] * slots_per + local_rank
    own_owner = lax.dynamic_index_in_dim(owners_all, seq_index, 0, keepdims=False)
    own_rank = lax.dynamic_index_in_dim(local_rank, seq_index, 0, keepdims=False)
    destination = own_owner * slots_per + own_rank
    send_table = (jnp.arange(cache_slots, dtype=jnp.int32)[:, None] == destination[None, :]).astype(
        jnp.bfloat16
    )
    page_rows = own_cols.reshape(pages_dev, PAGE * cache_width)
    outgoing_pages = jnp.dot(send_table, page_rows, preferred_element_type=jnp.float32).astype(
        jnp.bfloat16
    )
    outgoing_pages = outgoing_pages.reshape(seq_count, slots_per, PAGE * cache_width)
    arrived = lax.all_to_all(outgoing_pages, "seq", split_axis=0, concat_axis=0, tiled=True)
    owned_here = page_owner == seq_index
    place_table = (
        (page_slot[None, :] == jnp.arange(cache_slots, dtype=jnp.int32)[:, None])
        & owned_here[None, :]
    ).astype(jnp.bfloat16)
    pick_table = (
        column_of.reshape(-1)[:, None] == jnp.arange(cache_slots, dtype=jnp.int32)[None, :]
    ).astype(jnp.bfloat16)
    route_table = jnp.dot(place_table, pick_table, preferred_element_type=jnp.float32).astype(
        jnp.bfloat16
    )
    cache_local = jnp.dot(
        route_table,
        arrived.reshape(cache_slots, PAGE * cache_width),
        preferred_element_type=jnp.float32,
    )
    kv_cache = cache_local.astype(jnp.bfloat16).reshape(cache_slots * PAGE, cache_width)
    blocks_back = WINDOW // tok_rows
    pieces = []
    for distance in range(blocks_back, 0, -1):
        pieces.append(passed_along(key_value, "seq", distance))
    behind = jnp.concatenate(pieces, axis=0)
    band_all = jnp.concatenate([behind, key_value], axis=0).reshape(-1, kv_heads_dev, 2, HD)
    query_heads = queries.reshape(tok_rows, kv_heads_dev, heads_dev // kv_heads_dev, HD)
    block_rows = min(256, tok_rows)
    base_position = seq_index * tok_rows

    def one_block(block_idx, query_block):
        first_row = block_idx * block_rows
        band_block = lax.dynamic_slice_in_dim(band_all, first_row, WINDOW + block_rows, 0)
        starts = lax.dynamic_slice_in_dim(seg_start, first_row, block_rows, 0)
        positions_q = base_position + first_row + jnp.arange(block_rows, dtype=jnp.int32)
        positions_k = (
            base_position + first_row - WINDOW + jnp.arange(WINDOW + block_rows, dtype=jnp.int32)
        )
        return attend_band(query_block, band_block, positions_q, positions_k, starts)

    col_width = w_out.shape[1] // tp_count
    chips = tp_count // 2
    core = tp_index % 2
    chip = tp_index // 2
    swap_pairs = [(p, p ^ 1) for p in range(tp_count)]

    def reduce_in_chip(projected):
        rows = projected.shape[0]
        parts = projected.astype(jnp.bfloat16).reshape(rows, chips, 2, col_width)
        keep = lax.dynamic_index_in_dim(parts, core, 2, keepdims=False)
        send = lax.dynamic_index_in_dim(parts, 1 - core, 2, keepdims=False)
        got = lax.ppermute(send, "tp", swap_pairs)
        return (keep.astype(jnp.float32) + got.astype(jnp.float32)).astype(jnp.bfloat16)

    def reduce_across_chips(chip_sum):
        total = lax.dynamic_index_in_dim(chip_sum, chip, 1, keepdims=False).astype(jnp.float32)
        for shift in range(1, chips):
            piece = lax.dynamic_index_in_dim(chip_sum, (chip + shift) % chips, 1, keepdims=False)
            moved = lax.ppermute(
                piece, "tp", [(p, (p + 2 * shift) % tp_count) for p in range(tp_count)]
            )
            total = total + moved.astype(jnp.float32)
        return total.astype(jnp.bfloat16)

    n_blocks = tok_rows // block_rows
    chip_sums = [None] * n_blocks
    out_blocks = [None] * n_blocks
    for block_idx in range(n_blocks):
        query_block = query_heads[block_idx * block_rows:(block_idx + 1) * block_rows]
        if block_idx >= 1:
            earlier = out_blocks[block_idx - 2] if block_idx >= 2 else None
            chip_sums[block_idx - 1], earlier, query_block = lax.optimization_barrier(
                (chip_sums[block_idx - 1], earlier, query_block)
            )
            if block_idx >= 2:
                out_blocks[block_idx - 2] = earlier
            out_blocks[block_idx - 1] = reduce_across_chips(chip_sums[block_idx - 1])
        attended = one_block(block_idx, query_block).reshape(block_rows, heads_dev * HD)
        projected = jnp.dot(attended, w_out, preferred_element_type=jnp.float32)
        chip_sums[block_idx] = reduce_in_chip(projected)
    out_blocks[n_blocks - 1] = reduce_across_chips(chip_sums[n_blocks - 1])
    layer_out = jnp.concatenate(out_blocks, axis=0)
    return (layer_out, kv_cache)


def solution(mesh):
    return jax.shard_map(
        body,
        mesh=mesh,
        in_specs=(P("seq", None), P(None, "tp"), P(), P("tp", None), P("seq"), P(), P()),
        out_specs=(P("seq", "tp"), P("seq", "tp")),
        check_vma=False,
    )
```

```python
import jax
import jax.numpy as jnp
from jax import lax
from jax.sharding import PartitionSpec as P

H = 32
KVH = 4
HD = 64
WINDOW = 2048
PAGE = 16


masked_value = -1e30


def passed_along(value, axis, steps):
    count = lax.axis_size(axis)
    leading, last = (max(0, -steps), min(count, count - steps))
    return lax.ppermute(value, axis, [(source, source + steps) for source in range(leading, last)])


def attend_band(query_block, band_block, positions_q, positions_k, starts):
    keys_block = band_block[:, :, 0, :]
    values_block = band_block[:, :, 1, :]
    head_size = query_block.shape[-1]
    scores = jnp.einsum(
        "qkgd,ckd->kgqc", query_block, keys_block, preferred_element_type=jnp.float32
    ) * head_size ** (-0.5)
    lower_bound = jnp.maximum(starts, positions_q - WINDOW + 1)
    visible = (positions_k[None, :] >= lower_bound[:, None]) & (
        positions_k[None, :] <= positions_q[:, None]
    )
    scores = jnp.where(visible, scores, masked_value)
    largest = jnp.max(scores, axis=-1, keepdims=True)
    powered = jnp.exp(scores - largest)
    row_total = jnp.sum(powered, axis=-1, keepdims=True)
    weights = powered.astype(jnp.bfloat16)
    result = (
        jnp.einsum("kgqc,ckd->kgqd", weights, values_block, preferred_element_type=jnp.float32)
        / row_total
    )
    return jnp.transpose(result, (2, 0, 1, 3)).astype(jnp.bfloat16)


def body(tokens, w_query, w_kv, w_out, seg_start, page_owner, page_slot):
    seq_index = lax.axis_index("seq")
    tp_index = lax.axis_index("tp")
    seq_count = lax.axis_size("seq")
    tp_count = lax.axis_size("tp")
    tok_rows = tokens.shape[0]
    group_size = H // KVH
    heads_dev = H // tp_count
    kv_heads_dev = max(1, heads_dev // group_size)
    kv_width = kv_heads_dev * 2 * HD
    cache_width = KVH * 2 * HD // tp_count
    first_col = tp_index * heads_dev // group_size * 2 * HD
    queries = jnp.dot(tokens, w_query, preferred_element_type=jnp.float32).astype(jnp.bfloat16)
    w_local = lax.dynamic_slice_in_dim(w_kv, first_col, kv_width, 1)
    key_value = jnp.dot(tokens, w_local, preferred_element_type=jnp.float32).astype(jnp.bfloat16)
    own_cols = lax.dynamic_slice_in_dim(
        key_value, tp_index * cache_width - first_col, cache_width, 1
    )
    pages_dev = tok_rows // PAGE
    slots_per = max(2, 2 * pages_dev // seq_count)
    cache_slots = seq_count * slots_per
    owners_all = page_owner.reshape(seq_count, pages_dev)
    owner_hot = (
        owners_all[:, :, None] == jnp.arange(seq_count, dtype=jnp.int32)[None, None, :]
    ).astype(jnp.int32)
    local_rank = jnp.sum((jnp.cumsum(owner_hot, axis=1) - owner_hot) * owner_hot, axis=2)
    column_of = jnp.arange(seq_count, dtype=jnp.int32)[:, None] * slots_per + local_rank
    own_owner = lax.dynamic_index_in_dim(owners_all, seq_index, 0, keepdims=False)
    own_rank = lax.dynamic_index_in_dim(local_rank, seq_index, 0, keepdims=False)
    destination = own_owner * slots_per + own_rank
    send_table = (jnp.arange(cache_slots, dtype=jnp.int32)[:, None] == destination[None, :]).astype(
        jnp.bfloat16
    )
    page_rows = own_cols.reshape(pages_dev, PAGE * cache_width)
    outgoing_pages = jnp.dot(send_table, page_rows, preferred_element_type=jnp.float32).astype(
        jnp.bfloat16
    )
    outgoing_pages = outgoing_pages.reshape(seq_count, slots_per, PAGE * cache_width)
    arrived = lax.all_to_all(outgoing_pages, "seq", split_axis=0, concat_axis=0, tiled=True)
    owned_here = page_owner == seq_index
    place_table = (
        (page_slot[None, :] == jnp.arange(cache_slots, dtype=jnp.int32)[:, None])
        & owned_here[None, :]
    ).astype(jnp.bfloat16)
    pick_table = (
        column_of.reshape(-1)[:, None] == jnp.arange(cache_slots, dtype=jnp.int32)[None, :]
    ).astype(jnp.bfloat16)
    route_table = jnp.dot(place_table, pick_table, preferred_element_type=jnp.float32).astype(
        jnp.bfloat16
    )
    cache_local = jnp.dot(
        route_table,
        arrived.reshape(cache_slots, PAGE * cache_width),
        preferred_element_type=jnp.float32,
    )
    kv_cache = cache_local.astype(jnp.bfloat16).reshape(cache_slots * PAGE, cache_width)
    blocks_back = WINDOW // tok_rows
    pieces = []
    for distance in range(blocks_back, 0, -1):
        pieces.append(passed_along(key_value, "seq", distance))
    behind = jnp.concatenate(pieces, axis=0)
    band_all = jnp.concatenate([behind, key_value], axis=0).reshape(-1, kv_heads_dev, 2, HD)
    query_heads = queries.reshape(tok_rows, kv_heads_dev, heads_dev // kv_heads_dev, HD)
    block_rows = min(256, tok_rows)
    base_position = seq_index * tok_rows

    def one_block(block_idx, query_block):
        first_row = block_idx * block_rows
        band_block = lax.dynamic_slice_in_dim(band_all, first_row, WINDOW + block_rows, 0)
        starts = lax.dynamic_slice_in_dim(seg_start, first_row, block_rows, 0)
        positions_q = base_position + first_row + jnp.arange(block_rows, dtype=jnp.int32)
        positions_k = (
            base_position + first_row - WINDOW + jnp.arange(WINDOW + block_rows, dtype=jnp.int32)
        )
        return attend_band(query_block, band_block, positions_q, positions_k, starts)

    col_width = w_out.shape[1] // tp_count
    chips = tp_count // 2
    core = tp_index % 2
    chip = tp_index // 2
    swap_pairs = [(p, p ^ 1) for p in range(tp_count)]

    def reduce_in_chip(projected):
        rows = projected.shape[0]
        parts = projected.astype(jnp.bfloat16).reshape(rows, chips, 2, col_width)
        keep = lax.dynamic_index_in_dim(parts, core, 2, keepdims=False)
        send = lax.dynamic_index_in_dim(parts, 1 - core, 2, keepdims=False)
        got = lax.ppermute(send, "tp", swap_pairs)
        return (keep.astype(jnp.float32) + got.astype(jnp.float32)).astype(jnp.bfloat16)

    def reduce_across_chips(chip_sum):
        total = lax.dynamic_index_in_dim(chip_sum, chip, 1, keepdims=False).astype(jnp.float32)
        for shift in range(1, chips):
            piece = lax.dynamic_index_in_dim(chip_sum, (chip + shift) % chips, 1, keepdims=False)
            moved = lax.ppermute(
                piece, "tp", [(p, (p + 2 * shift) % tp_count) for p in range(tp_count)]
            )
            total = total + moved.astype(jnp.float32)
        return total.astype(jnp.bfloat16)

    n_blocks = tok_rows // block_rows
    per_chunk = max(1, n_blocks // 2)
    n_chunks = n_blocks // per_chunk
    chip_sums = [None] * n_chunks
    out_blocks = [None] * n_chunks
    projected_rows = []
    for block_idx in range(n_blocks):
        chunk_idx, within = divmod(block_idx, per_chunk)
        query_block = query_heads[block_idx * block_rows:(block_idx + 1) * block_rows]
        if within == 0 and chunk_idx >= 1:
            chip_sums[chunk_idx - 1], query_block = lax.optimization_barrier(
                (chip_sums[chunk_idx - 1], query_block)
            )
            out_blocks[chunk_idx - 1] = reduce_across_chips(chip_sums[chunk_idx - 1])
        if within == 1 and chunk_idx >= 1:
            out_blocks[chunk_idx - 1], query_block = lax.optimization_barrier(
                (out_blocks[chunk_idx - 1], query_block)
            )
        attended = one_block(block_idx, query_block).reshape(block_rows, heads_dev * HD)
        projected_rows.append(jnp.dot(attended, w_out, preferred_element_type=jnp.float32))
        if within == per_chunk - 1:
            chip_sums[chunk_idx] = reduce_in_chip(jnp.concatenate(projected_rows, axis=0))
            projected_rows = []
    out_blocks[n_chunks - 1] = reduce_across_chips(chip_sums[n_chunks - 1])
    layer_out = jnp.concatenate(out_blocks, axis=0)
    return (layer_out, kv_cache)


def solution(mesh):
    return jax.shard_map(
        body,
        mesh=mesh,
        in_specs=(P("seq", None), P(None, "tp"), P(), P("tp", None), P("seq"), P(), P()),
        out_specs=(P("seq", "tp"), P("seq", "tp")),
        check_vma=False,
    )
```

```python
import jax
import jax.numpy as jnp
from jax import lax
from jax.sharding import PartitionSpec as P

H = 32
KVH = 4
HD = 64
WINDOW = 2048
PAGE = 16


masked_value = -1e30


def passed_along(value, axis, steps):
    count = lax.axis_size(axis)
    leading, last = (max(0, -steps), min(count, count - steps))
    return lax.ppermute(value, axis, [(source, source + steps) for source in range(leading, last)])


def attend_band(query_block, band_block, positions_q, positions_k, starts):
    keys_block = band_block[:, :, 0, :]
    values_block = band_block[:, :, 1, :]
    head_size = query_block.shape[-1]
    scores = jnp.einsum(
        "qkgd,ckd->kgqc", query_block, keys_block, preferred_element_type=jnp.float32
    ) * head_size ** (-0.5)
    lower_bound = jnp.maximum(starts, positions_q - WINDOW + 1)
    visible = (positions_k[None, :] >= lower_bound[:, None]) & (
        positions_k[None, :] <= positions_q[:, None]
    )
    scores = jnp.where(visible, scores, masked_value)
    largest = jnp.max(scores, axis=-1, keepdims=True)
    powered = jnp.exp(scores - largest)
    row_total = jnp.sum(powered, axis=-1, keepdims=True)
    weights = powered.astype(jnp.bfloat16)
    result = (
        jnp.einsum("kgqc,ckd->kgqd", weights, values_block, preferred_element_type=jnp.float32)
        / row_total
    )
    return jnp.transpose(result, (2, 0, 1, 3)).astype(jnp.bfloat16)


def body(tokens, w_query, w_kv, w_out, seg_start, page_owner, page_slot):
    seq_index = lax.axis_index("seq")
    tp_index = lax.axis_index("tp")
    seq_count = lax.axis_size("seq")
    tp_count = lax.axis_size("tp")
    tok_rows = tokens.shape[0]
    group_size = H // KVH
    heads_dev = H // tp_count
    kv_heads_dev = max(1, heads_dev // group_size)
    kv_width = kv_heads_dev * 2 * HD
    cache_width = KVH * 2 * HD // tp_count
    first_col = tp_index * heads_dev // group_size * 2 * HD
    queries = jnp.dot(tokens, w_query, preferred_element_type=jnp.float32).astype(jnp.bfloat16)
    w_local = lax.dynamic_slice_in_dim(w_kv, first_col, kv_width, 1)
    key_value = jnp.dot(tokens, w_local, preferred_element_type=jnp.float32).astype(jnp.bfloat16)
    own_cols = lax.dynamic_slice_in_dim(
        key_value, tp_index * cache_width - first_col, cache_width, 1
    )
    def write_cache(own_cols):
        pages_dev = tok_rows // PAGE
        slots_per = max(2, 2 * pages_dev // seq_count)
        cache_slots = seq_count * slots_per
        owners_all = page_owner.reshape(seq_count, pages_dev)
        owner_hot = (
            owners_all[:, :, None] == jnp.arange(seq_count, dtype=jnp.int32)[None, None, :]
        ).astype(jnp.int32)
        local_rank = jnp.sum((jnp.cumsum(owner_hot, axis=1) - owner_hot) * owner_hot, axis=2)
        column_of = jnp.arange(seq_count, dtype=jnp.int32)[:, None] * slots_per + local_rank
        own_owner = lax.dynamic_index_in_dim(owners_all, seq_index, 0, keepdims=False)
        own_rank = lax.dynamic_index_in_dim(local_rank, seq_index, 0, keepdims=False)
        destination = own_owner * slots_per + own_rank
        send_table = (jnp.arange(cache_slots, dtype=jnp.int32)[:, None] == destination[None, :]).astype(
            jnp.bfloat16
        )
        page_rows = own_cols.reshape(pages_dev, PAGE * cache_width)
        outgoing_pages = jnp.dot(send_table, page_rows, preferred_element_type=jnp.float32).astype(
            jnp.bfloat16
        )
        outgoing_pages = outgoing_pages.reshape(seq_count, slots_per, PAGE * cache_width)
        arrived = lax.all_to_all(outgoing_pages, "seq", split_axis=0, concat_axis=0, tiled=True)
        owned_here = page_owner == seq_index
        place_table = (
            (page_slot[None, :] == jnp.arange(cache_slots, dtype=jnp.int32)[:, None])
            & owned_here[None, :]
        ).astype(jnp.bfloat16)
        pick_table = (
            column_of.reshape(-1)[:, None] == jnp.arange(cache_slots, dtype=jnp.int32)[None, :]
        ).astype(jnp.bfloat16)
        route_table = jnp.dot(place_table, pick_table, preferred_element_type=jnp.float32).astype(
            jnp.bfloat16
        )
        cache_local = jnp.dot(
            route_table,
            arrived.reshape(cache_slots, PAGE * cache_width),
            preferred_element_type=jnp.float32,
        )
        kv_cache = cache_local.astype(jnp.bfloat16).reshape(cache_slots * PAGE, cache_width)
        return kv_cache

    blocks_back = WINDOW // tok_rows
    pieces = []
    for distance in range(blocks_back, 0, -1):
        pieces.append(passed_along(key_value, "seq", distance))
    behind = jnp.concatenate(pieces, axis=0)
    band_all = jnp.concatenate([behind, key_value], axis=0).reshape(-1, kv_heads_dev, 2, HD)
    query_heads = queries.reshape(tok_rows, kv_heads_dev, heads_dev // kv_heads_dev, HD)
    block_rows = min(256, tok_rows)
    base_position = seq_index * tok_rows

    def one_block(block_idx, query_block):
        first_row = block_idx * block_rows
        band_block = lax.dynamic_slice_in_dim(band_all, first_row, WINDOW + block_rows, 0)
        starts = lax.dynamic_slice_in_dim(seg_start, first_row, block_rows, 0)
        positions_q = base_position + first_row + jnp.arange(block_rows, dtype=jnp.int32)
        positions_k = (
            base_position + first_row - WINDOW + jnp.arange(WINDOW + block_rows, dtype=jnp.int32)
        )
        return attend_band(query_block, band_block, positions_q, positions_k, starts)

    col_width = w_out.shape[1] // tp_count
    chips = tp_count // 2
    core = tp_index % 2
    chip = tp_index // 2
    swap_pairs = [(p, p ^ 1) for p in range(tp_count)]

    def reduce_in_chip(projected):
        rows = projected.shape[0]
        parts = projected.astype(jnp.bfloat16).reshape(rows, chips, 2, col_width)
        keep = lax.dynamic_index_in_dim(parts, core, 2, keepdims=False)
        send = lax.dynamic_index_in_dim(parts, 1 - core, 2, keepdims=False)
        got = lax.ppermute(send, "tp", swap_pairs)
        return (keep.astype(jnp.float32) + got.astype(jnp.float32)).astype(jnp.bfloat16)

    def reduce_across_chips(chip_sum):
        total = lax.dynamic_index_in_dim(chip_sum, chip, 1, keepdims=False).astype(jnp.float32)
        for shift in range(1, chips):
            piece = lax.dynamic_index_in_dim(chip_sum, (chip + shift) % chips, 1, keepdims=False)
            moved = lax.ppermute(
                piece, "tp", [(p, (p + 2 * shift) % tp_count) for p in range(tp_count)]
            )
            total = total + moved.astype(jnp.float32)
        return total.astype(jnp.bfloat16)

    n_blocks = tok_rows // block_rows
    chip_sums = [None] * n_blocks
    out_blocks = [None] * n_blocks
    for block_idx in range(n_blocks):
        query_block = query_heads[block_idx * block_rows:(block_idx + 1) * block_rows]
        if block_idx >= 1:
            earlier = out_blocks[block_idx - 2] if block_idx >= 2 else None
            chip_sums[block_idx - 1], earlier, query_block = lax.optimization_barrier(
                (chip_sums[block_idx - 1], earlier, query_block)
            )
            if block_idx >= 2:
                out_blocks[block_idx - 2] = earlier
            out_blocks[block_idx - 1] = reduce_across_chips(chip_sums[block_idx - 1])
        attended = one_block(block_idx, query_block).reshape(block_rows, heads_dev * HD)
        projected = jnp.dot(attended, w_out, preferred_element_type=jnp.float32)
        chip_sums[block_idx] = reduce_in_chip(projected)
    own_cols, chip_sums[n_blocks - 1] = lax.optimization_barrier(
        (own_cols, chip_sums[n_blocks - 1])
    )
    out_blocks[n_blocks - 1] = reduce_across_chips(chip_sums[n_blocks - 1])
    kv_cache = write_cache(own_cols)
    layer_out = jnp.concatenate(out_blocks, axis=0)
    return (layer_out, kv_cache)


def solution(mesh):
    return jax.shard_map(
        body,
        mesh=mesh,
        in_specs=(P("seq", None), P(None, "tp"), P(), P("tp", None), P("seq"), P(), P()),
        out_specs=(P("seq", "tp"), P("seq", "tp")),
        check_vma=False,
    )
```

```python
import jax
import jax.numpy as jnp
from jax import lax
from jax.sharding import PartitionSpec as P

H = 32
KVH = 4
HD = 64
WINDOW = 2048
PAGE = 16


masked_value = -1e30


def passed_along(value, axis, steps):
    count = lax.axis_size(axis)
    leading, last = (max(0, -steps), min(count, count - steps))
    return lax.ppermute(value, axis, [(source, source + steps) for source in range(leading, last)])


def attend_band(query_block, band_block, positions_q, positions_k, starts):
    keys_block = band_block[:, :, 0, :]
    values_block = band_block[:, :, 1, :]
    head_size = query_block.shape[-1]
    scores = jnp.einsum(
        "qkgd,ckd->kgqc", query_block, keys_block, preferred_element_type=jnp.float32
    ) * head_size ** (-0.5)
    lower_bound = jnp.maximum(starts, positions_q - WINDOW + 1)
    visible = (positions_k[None, :] >= lower_bound[:, None]) & (
        positions_k[None, :] <= positions_q[:, None]
    )
    scores = jnp.where(visible, scores, masked_value)
    largest = jnp.max(scores, axis=-1, keepdims=True)
    powered = jnp.exp(scores - largest)
    row_total = jnp.sum(powered, axis=-1, keepdims=True)
    weights = powered.astype(jnp.bfloat16)
    result = (
        jnp.einsum("kgqc,ckd->kgqd", weights, values_block, preferred_element_type=jnp.float32)
        / row_total
    )
    return jnp.transpose(result, (2, 0, 1, 3)).astype(jnp.bfloat16)


def body(tokens, w_query, w_kv, w_out, seg_start, page_owner, page_slot):
    seq_index = lax.axis_index("seq")
    tp_index = lax.axis_index("tp")
    seq_count = lax.axis_size("seq")
    tp_count = lax.axis_size("tp")
    tok_rows = tokens.shape[0]
    group_size = H // KVH
    heads_dev = H // tp_count
    kv_heads_dev = max(1, heads_dev // group_size)
    kv_width = kv_heads_dev * 2 * HD
    cache_width = KVH * 2 * HD // tp_count
    first_col = tp_index * heads_dev // group_size * 2 * HD
    queries = jnp.dot(tokens, w_query, preferred_element_type=jnp.float32).astype(jnp.bfloat16)
    w_local = lax.dynamic_slice_in_dim(w_kv, first_col, kv_width, 1)
    key_value = jnp.dot(tokens, w_local, preferred_element_type=jnp.float32).astype(jnp.bfloat16)
    own_cols = lax.dynamic_slice_in_dim(
        key_value, tp_index * cache_width - first_col, cache_width, 1
    )
    def write_cache(own_cols):
        pages_dev = tok_rows // PAGE
        slots_per = max(2, 2 * pages_dev // seq_count)
        cache_slots = seq_count * slots_per
        owners_all = page_owner.reshape(seq_count, pages_dev)
        owner_hot = (
            owners_all[:, :, None] == jnp.arange(seq_count, dtype=jnp.int32)[None, None, :]
        ).astype(jnp.int32)
        local_rank = jnp.sum((jnp.cumsum(owner_hot, axis=1) - owner_hot) * owner_hot, axis=2)
        column_of = jnp.arange(seq_count, dtype=jnp.int32)[:, None] * slots_per + local_rank
        own_owner = lax.dynamic_index_in_dim(owners_all, seq_index, 0, keepdims=False)
        own_rank = lax.dynamic_index_in_dim(local_rank, seq_index, 0, keepdims=False)
        destination = own_owner * slots_per + own_rank
        send_table = (jnp.arange(cache_slots, dtype=jnp.int32)[:, None] == destination[None, :]).astype(
            jnp.bfloat16
        )
        page_rows = own_cols.reshape(pages_dev, PAGE * cache_width)
        outgoing_pages = jnp.dot(send_table, page_rows, preferred_element_type=jnp.float32).astype(
            jnp.bfloat16
        )
        outgoing_pages = outgoing_pages.reshape(seq_count, slots_per, PAGE * cache_width)
        arrived = lax.all_to_all(outgoing_pages, "seq", split_axis=0, concat_axis=0, tiled=True)
        owned_here = page_owner == seq_index
        place_table = (
            (page_slot[None, :] == jnp.arange(cache_slots, dtype=jnp.int32)[:, None])
            & owned_here[None, :]
        ).astype(jnp.bfloat16)
        pick_table = (
            column_of.reshape(-1)[:, None] == jnp.arange(cache_slots, dtype=jnp.int32)[None, :]
        ).astype(jnp.bfloat16)
        route_table = jnp.dot(place_table, pick_table, preferred_element_type=jnp.float32).astype(
            jnp.bfloat16
        )
        cache_local = jnp.dot(
            route_table,
            arrived.reshape(cache_slots, PAGE * cache_width),
            preferred_element_type=jnp.float32,
        )
        kv_cache = cache_local.astype(jnp.bfloat16).reshape(cache_slots * PAGE, cache_width)
        return kv_cache

    blocks_back = WINDOW // tok_rows
    pieces = []
    for distance in range(blocks_back, 0, -1):
        pieces.append(passed_along(key_value, "seq", distance))
    behind = jnp.concatenate(pieces, axis=0)
    band_all = jnp.concatenate([behind, key_value], axis=0).reshape(-1, kv_heads_dev, 2, HD)
    query_heads = queries.reshape(tok_rows, kv_heads_dev, heads_dev // kv_heads_dev, HD)
    block_rows = min(256, tok_rows)
    base_position = seq_index * tok_rows

    def one_block(block_idx, query_block):
        first_row = block_idx * block_rows
        band_block = lax.dynamic_slice_in_dim(band_all, first_row, WINDOW + block_rows, 0)
        starts = lax.dynamic_slice_in_dim(seg_start, first_row, block_rows, 0)
        positions_q = base_position + first_row + jnp.arange(block_rows, dtype=jnp.int32)
        positions_k = (
            base_position + first_row - WINDOW + jnp.arange(WINDOW + block_rows, dtype=jnp.int32)
        )
        return attend_band(query_block, band_block, positions_q, positions_k, starts)

    col_width = w_out.shape[1] // tp_count
    chips = tp_count // 2
    core = tp_index % 2
    chip = tp_index // 2
    swap_pairs = [(p, p ^ 1) for p in range(tp_count)]

    def reduce_in_chip(projected):
        rows = projected.shape[0]
        parts = projected.astype(jnp.bfloat16).reshape(rows, chips, 2, col_width)
        keep = lax.dynamic_index_in_dim(parts, core, 2, keepdims=False)
        send = lax.dynamic_index_in_dim(parts, 1 - core, 2, keepdims=False)
        got = lax.ppermute(send, "tp", swap_pairs)
        return (keep.astype(jnp.float32) + got.astype(jnp.float32)).astype(jnp.bfloat16)

    def reduce_across_chips(chip_sum):
        total = lax.dynamic_index_in_dim(chip_sum, chip, 1, keepdims=False).astype(jnp.float32)
        for shift in range(1, chips):
            piece = lax.dynamic_index_in_dim(chip_sum, (chip + shift) % chips, 1, keepdims=False)
            moved = lax.ppermute(
                piece, "tp", [(p, (p + 2 * shift) % tp_count) for p in range(tp_count)]
            )
            total = total + moved.astype(jnp.float32)
        return total.astype(jnp.bfloat16)

    n_blocks = tok_rows // block_rows

    def block_sum(block_idx, prev_sum=None):
        query_block = lax.dynamic_slice_in_dim(query_heads, block_idx * block_rows, block_rows, 0)
        half = query_block.shape[2] // 2
        first = one_block(block_idx, query_block[:, :, :half])
        second_query = query_block[:, :, half:]
        total_prev = None
        if prev_sum is not None:
            total_prev, second_query = lax.optimization_barrier(
                (reduce_across_chips(prev_sum), second_query)
            )
        second = one_block(block_idx, second_query)
        attended = jnp.concatenate([first, second], axis=2).reshape(block_rows, heads_dev * HD)
        projected = jnp.dot(attended, w_out, preferred_element_type=jnp.float32)
        return reduce_in_chip(projected), total_prev

    def step(prev_sum, block_idx):
        return block_sum(block_idx, prev_sum)

    last_sum, earlier = lax.scan(
        step, block_sum(jnp.int32(0))[0], jnp.arange(1, n_blocks, dtype=jnp.int32)
    )
    own_cols, last_sum = lax.optimization_barrier((own_cols, last_sum))
    out_blocks = [earlier.reshape(-1, col_width), reduce_across_chips(last_sum)]
    kv_cache = write_cache(own_cols)
    layer_out = jnp.concatenate(out_blocks, axis=0)
    return (layer_out, kv_cache)


def solution(mesh):
    return jax.shard_map(
        body,
        mesh=mesh,
        in_specs=(P("seq", None), P(None, "tp"), P(), P("tp", None), P("seq"), P(), P()),
        out_specs=(P("seq", "tp"), P("seq", "tp")),
        check_vma=False,
    )
```

```python
import jax
import jax.numpy as jnp
from jax import lax
from jax.sharding import PartitionSpec as P

H = 32
KVH = 4
HD = 64
WINDOW = 2048
PAGE = 16


masked_value = -1e30


def passed_along(value, axis, steps):
    count = lax.axis_size(axis)
    leading, last = (max(0, -steps), min(count, count - steps))
    return lax.ppermute(value, axis, [(source, source + steps) for source in range(leading, last)])


def attend_band(query_block, band_block, positions_q, positions_k, starts):
    keys_block = band_block[:, :, 0, :]
    values_block = band_block[:, :, 1, :]
    head_size = query_block.shape[-1]
    scores = jnp.einsum(
        "qkgd,ckd->kgqc", query_block, keys_block, preferred_element_type=jnp.float32
    ) * head_size ** (-0.5)
    lower_bound = jnp.maximum(starts, positions_q - WINDOW + 1)
    visible = (positions_k[None, :] >= lower_bound[:, None]) & (
        positions_k[None, :] <= positions_q[:, None]
    )
    scores = jnp.where(visible, scores, masked_value)
    largest = jnp.max(scores, axis=-1, keepdims=True)
    powered = jnp.exp(scores - largest)
    row_total = jnp.sum(powered, axis=-1, keepdims=True)
    weights = powered.astype(jnp.bfloat16)
    result = (
        jnp.einsum("kgqc,ckd->kgqd", weights, values_block, preferred_element_type=jnp.float32)
        / row_total
    )
    return jnp.transpose(result, (2, 0, 1, 3)).astype(jnp.bfloat16)


def body(tokens, w_query, w_kv, w_out, seg_start, page_owner, page_slot):
    seq_index = lax.axis_index("seq")
    tp_index = lax.axis_index("tp")
    seq_count = lax.axis_size("seq")
    tp_count = lax.axis_size("tp")
    tok_rows = tokens.shape[0]
    group_size = H // KVH
    heads_dev = H // tp_count
    kv_heads_dev = max(1, heads_dev // group_size)
    kv_width = kv_heads_dev * 2 * HD
    cache_width = KVH * 2 * HD // tp_count
    first_col = tp_index * heads_dev // group_size * 2 * HD
    queries = jnp.dot(tokens, w_query, preferred_element_type=jnp.float32).astype(jnp.bfloat16)
    w_local = lax.dynamic_slice_in_dim(w_kv, first_col, kv_width, 1)
    key_value = jnp.dot(tokens, w_local, preferred_element_type=jnp.float32).astype(jnp.bfloat16)
    own_cols = lax.dynamic_slice_in_dim(
        key_value, tp_index * cache_width - first_col, cache_width, 1
    )
    def write_cache(own_cols):
        pages_dev = tok_rows // PAGE
        slots_per = max(2, 2 * pages_dev // seq_count)
        cache_slots = seq_count * slots_per
        owners_all = page_owner.reshape(seq_count, pages_dev)
        owner_hot = (
            owners_all[:, :, None] == jnp.arange(seq_count, dtype=jnp.int32)[None, None, :]
        ).astype(jnp.int32)
        local_rank = jnp.sum((jnp.cumsum(owner_hot, axis=1) - owner_hot) * owner_hot, axis=2)
        column_of = jnp.arange(seq_count, dtype=jnp.int32)[:, None] * slots_per + local_rank
        own_owner = lax.dynamic_index_in_dim(owners_all, seq_index, 0, keepdims=False)
        own_rank = lax.dynamic_index_in_dim(local_rank, seq_index, 0, keepdims=False)
        destination = own_owner * slots_per + own_rank
        send_table = (jnp.arange(cache_slots, dtype=jnp.int32)[:, None] == destination[None, :]).astype(
            jnp.bfloat16
        )
        page_rows = own_cols.reshape(pages_dev, PAGE * cache_width)
        outgoing_pages = jnp.dot(send_table, page_rows, preferred_element_type=jnp.float32).astype(
            jnp.bfloat16
        )
        outgoing_pages = outgoing_pages.reshape(seq_count, slots_per, PAGE * cache_width)
        arrived = lax.all_to_all(outgoing_pages, "seq", split_axis=0, concat_axis=0, tiled=True)
        owned_here = page_owner == seq_index
        place_table = (
            (page_slot[None, :] == jnp.arange(cache_slots, dtype=jnp.int32)[:, None])
            & owned_here[None, :]
        ).astype(jnp.bfloat16)
        pick_table = (
            column_of.reshape(-1)[:, None] == jnp.arange(cache_slots, dtype=jnp.int32)[None, :]
        ).astype(jnp.bfloat16)
        route_table = jnp.dot(place_table, pick_table, preferred_element_type=jnp.float32).astype(
            jnp.bfloat16
        )
        cache_local = jnp.dot(
            route_table,
            arrived.reshape(cache_slots, PAGE * cache_width),
            preferred_element_type=jnp.float32,
        )
        kv_cache = cache_local.astype(jnp.bfloat16).reshape(cache_slots * PAGE, cache_width)
        return kv_cache

    blocks_back = WINDOW // tok_rows
    pieces = []
    for distance in range(blocks_back, 0, -1):
        pieces.append(passed_along(key_value, "seq", distance))
    behind = jnp.concatenate(pieces, axis=0)
    band_all = jnp.concatenate([behind, key_value], axis=0).reshape(-1, kv_heads_dev, 2, HD)
    query_heads = queries.reshape(tok_rows, kv_heads_dev, heads_dev // kv_heads_dev, HD)
    block_rows = min(256, tok_rows)
    base_position = seq_index * tok_rows

    def one_block(block_idx, query_block):
        first_row = block_idx * block_rows
        band_block = lax.dynamic_slice_in_dim(band_all, first_row, WINDOW + block_rows, 0)
        starts = lax.dynamic_slice_in_dim(seg_start, first_row, block_rows, 0)
        positions_q = base_position + first_row + jnp.arange(block_rows, dtype=jnp.int32)
        positions_k = (
            base_position + first_row - WINDOW + jnp.arange(WINDOW + block_rows, dtype=jnp.int32)
        )
        return attend_band(query_block, band_block, positions_q, positions_k, starts)

    col_width = w_out.shape[1] // tp_count
    chips = tp_count // 2
    core = tp_index % 2
    chip = tp_index // 2
    swap_pairs = [(p, p ^ 1) for p in range(tp_count)]

    def reduce_in_chip(projected):
        rows = projected.shape[0]
        parts = projected.astype(jnp.bfloat16).reshape(rows, chips, 2, col_width)
        keep = lax.dynamic_index_in_dim(parts, core, 2, keepdims=False)
        send = lax.dynamic_index_in_dim(parts, 1 - core, 2, keepdims=False)
        got = lax.ppermute(send, "tp", swap_pairs)
        return (keep.astype(jnp.float32) + got.astype(jnp.float32)).astype(jnp.bfloat16)

    def reduce_across_chips(chip_sum):
        total = lax.dynamic_index_in_dim(chip_sum, chip, 1, keepdims=False).astype(jnp.float32)
        for shift in range(1, chips):
            piece = lax.dynamic_index_in_dim(chip_sum, (chip + shift) % chips, 1, keepdims=False)
            moved = lax.ppermute(
                piece, "tp", [(p, (p + 2 * shift) % tp_count) for p in range(tp_count)]
            )
            total = total + moved.astype(jnp.float32)
        return total.astype(jnp.bfloat16)

    n_blocks = tok_rows // block_rows
    chip_sums = [None] * n_blocks
    out_blocks = [None] * n_blocks
    for block_idx in range(n_blocks):
        query_block = query_heads[block_idx * block_rows:(block_idx + 1) * block_rows]
        if block_idx >= 1:
            chip_sums[block_idx - 1], query_block = lax.optimization_barrier(
                (chip_sums[block_idx - 1], query_block)
            )
        half = query_block.shape[2] // 2
        first = one_block(block_idx, query_block[:, :, :half])
        second_query = query_block[:, :, half:]
        if block_idx >= 1:
            out_blocks[block_idx - 1], second_query = lax.optimization_barrier(
                (reduce_across_chips(chip_sums[block_idx - 1]), second_query)
            )
        second = one_block(block_idx, second_query)
        attended = jnp.concatenate([first, second], axis=2).reshape(block_rows, heads_dev * HD)
        projected = jnp.dot(attended, w_out, preferred_element_type=jnp.float32)
        chip_sums[block_idx] = reduce_in_chip(projected)
    own_cols, chip_sums[n_blocks - 1] = lax.optimization_barrier(
        (own_cols, chip_sums[n_blocks - 1])
    )
    out_blocks[n_blocks - 1] = reduce_across_chips(chip_sums[n_blocks - 1])
    kv_cache = write_cache(own_cols)
    layer_out = jnp.concatenate(out_blocks, axis=0)
    return (layer_out, kv_cache)


def solution(mesh):
    return jax.shard_map(
        body,
        mesh=mesh,
        in_specs=(P("seq", None), P(None, "tp"), P(), P("tp", None), P("seq"), P(), P()),
        out_specs=(P("seq", "tp"), P("seq", "tp")),
        check_vma=False,
    )
```

```python
import jax
import jax.numpy as jnp
from jax import lax
from jax.sharding import PartitionSpec as P

H = 32
KVH = 4
HD = 64
WINDOW = 2048
PAGE = 16


masked_value = -1e30


def passed_along(value, axis, steps):
    count = lax.axis_size(axis)
    leading, last = (max(0, -steps), min(count, count - steps))
    return lax.ppermute(value, axis, [(source, source + steps) for source in range(leading, last)])


def attend_band(query_block, band_block, positions_q, positions_k, starts):
    keys_block = band_block[:, :, 0, :]
    values_block = band_block[:, :, 1, :]
    head_size = query_block.shape[-1]
    scores = jnp.einsum(
        "qkgd,ckd->kgqc", query_block, keys_block, preferred_element_type=jnp.float32
    ) * head_size ** (-0.5)
    lower_bound = jnp.maximum(starts, positions_q - WINDOW + 1)
    visible = (positions_k[None, :] >= lower_bound[:, None]) & (
        positions_k[None, :] <= positions_q[:, None]
    )
    scores = jnp.where(visible, scores, masked_value)
    largest = jnp.max(scores, axis=-1, keepdims=True)
    powered = jnp.exp(scores - largest)
    row_total = jnp.sum(powered, axis=-1, keepdims=True)
    weights = powered.astype(jnp.bfloat16)
    result = (
        jnp.einsum("kgqc,ckd->kgqd", weights, values_block, preferred_element_type=jnp.float32)
        / row_total
    )
    return jnp.transpose(result, (2, 0, 1, 3)).astype(jnp.bfloat16)


def body(tokens, w_query, w_kv, w_out, seg_start, page_owner, page_slot):
    seq_index = lax.axis_index("seq")
    tp_index = lax.axis_index("tp")
    seq_count = lax.axis_size("seq")
    tp_count = lax.axis_size("tp")
    tok_rows = tokens.shape[0]
    group_size = H // KVH
    heads_dev = H // tp_count
    kv_heads_dev = max(1, heads_dev // group_size)
    kv_width = kv_heads_dev * 2 * HD
    cache_width = KVH * 2 * HD // tp_count
    first_col = tp_index * heads_dev // group_size * 2 * HD
    queries = jnp.dot(tokens, w_query, preferred_element_type=jnp.float32).astype(jnp.bfloat16)
    w_local = lax.dynamic_slice_in_dim(w_kv, first_col, kv_width, 1)
    key_value = jnp.dot(tokens, w_local, preferred_element_type=jnp.float32).astype(jnp.bfloat16)
    own_cols = lax.dynamic_slice_in_dim(
        key_value, tp_index * cache_width - first_col, cache_width, 1
    )
    def write_cache(own_cols):
        pages_dev = tok_rows // PAGE
        slots_per = max(2, 2 * pages_dev // seq_count)
        cache_slots = seq_count * slots_per
        owners_all = page_owner.reshape(seq_count, pages_dev)
        owner_hot = (
            owners_all[:, :, None] == jnp.arange(seq_count, dtype=jnp.int32)[None, None, :]
        ).astype(jnp.int32)
        local_rank = jnp.sum((jnp.cumsum(owner_hot, axis=1) - owner_hot) * owner_hot, axis=2)
        column_of = jnp.arange(seq_count, dtype=jnp.int32)[:, None] * slots_per + local_rank
        own_owner = lax.dynamic_index_in_dim(owners_all, seq_index, 0, keepdims=False)
        own_rank = lax.dynamic_index_in_dim(local_rank, seq_index, 0, keepdims=False)
        destination = own_owner * slots_per + own_rank
        send_table = (jnp.arange(cache_slots, dtype=jnp.int32)[:, None] == destination[None, :]).astype(
            jnp.bfloat16
        )
        page_rows = own_cols.reshape(pages_dev, PAGE * cache_width)
        outgoing_pages = jnp.dot(send_table, page_rows, preferred_element_type=jnp.float32).astype(
            jnp.bfloat16
        )
        outgoing_pages = outgoing_pages.reshape(seq_count, slots_per, PAGE * cache_width)
        arrived = lax.all_to_all(outgoing_pages, "seq", split_axis=0, concat_axis=0, tiled=True)
        owned_here = page_owner == seq_index
        place_table = (
            (page_slot[None, :] == jnp.arange(cache_slots, dtype=jnp.int32)[:, None])
            & owned_here[None, :]
        ).astype(jnp.bfloat16)
        pick_table = (
            column_of.reshape(-1)[:, None] == jnp.arange(cache_slots, dtype=jnp.int32)[None, :]
        ).astype(jnp.bfloat16)
        route_table = jnp.dot(place_table, pick_table, preferred_element_type=jnp.float32).astype(
            jnp.bfloat16
        )
        cache_local = jnp.dot(
            route_table,
            arrived.reshape(cache_slots, PAGE * cache_width),
            preferred_element_type=jnp.float32,
        )
        kv_cache = cache_local.astype(jnp.bfloat16).reshape(cache_slots * PAGE, cache_width)
        return kv_cache

    blocks_back = WINDOW // tok_rows
    pieces = []
    for distance in range(blocks_back, 0, -1):
        pieces.append(passed_along(key_value, "seq", distance))
    behind = jnp.concatenate(pieces, axis=0)
    band_all = jnp.concatenate([behind, key_value], axis=0).reshape(-1, kv_heads_dev, 2, HD)
    query_heads = queries.reshape(tok_rows, kv_heads_dev, heads_dev // kv_heads_dev, HD)
    block_rows = min(256, tok_rows)
    base_position = seq_index * tok_rows

    def one_block(block_idx, query_block):
        first_row = block_idx * block_rows
        band_block = lax.dynamic_slice_in_dim(band_all, first_row, WINDOW + block_rows, 0)
        starts = lax.dynamic_slice_in_dim(seg_start, first_row, block_rows, 0)
        positions_q = base_position + first_row + jnp.arange(block_rows, dtype=jnp.int32)
        positions_k = (
            base_position + first_row - WINDOW + jnp.arange(WINDOW + block_rows, dtype=jnp.int32)
        )
        return attend_band(query_block, band_block, positions_q, positions_k, starts)

    col_width = w_out.shape[1] // tp_count
    chips = tp_count // 2
    core = tp_index % 2
    chip = tp_index // 2
    swap_pairs = [(p, p ^ 1) for p in range(tp_count)]

    w_parts = w_out.reshape(w_out.shape[0], chips, 2, col_width)

    def by_shift(which):
        picked = lax.dynamic_index_in_dim(w_parts, which, 2, keepdims=False)
        doubled = jnp.concatenate([picked, picked], axis=1)
        rolled = lax.dynamic_slice_in_dim(doubled, chip, chips, 1)
        return jnp.transpose(rolled, (1, 0, 2))

    w_keep = by_shift(core)
    w_send = by_shift(1 - core)

    def reduce_in_chip(attended):
        keep = jnp.einsum("rk,jkc->jrc", attended, w_keep, preferred_element_type=jnp.float32)
        send = jnp.einsum("rk,jkc->jrc", attended, w_send, preferred_element_type=jnp.float32)
        got = lax.ppermute(send.astype(jnp.bfloat16), "tp", swap_pairs)
        keep = keep.astype(jnp.bfloat16).astype(jnp.float32)
        return (keep + got.astype(jnp.float32)).astype(jnp.bfloat16)

    def reduce_across_chips(chip_sum):
        total = chip_sum[0].astype(jnp.float32)
        for shift in range(1, chips):
            moved = lax.ppermute(
                chip_sum[shift], "tp", [(p, (p + 2 * shift) % tp_count) for p in range(tp_count)]
            )
            total = total + moved.astype(jnp.float32)
        return total.astype(jnp.bfloat16)

    n_blocks = tok_rows // block_rows
    chip_sums = [None] * n_blocks
    out_blocks = [None] * n_blocks
    for block_idx in range(n_blocks):
        query_block = query_heads[block_idx * block_rows:(block_idx + 1) * block_rows]
        if block_idx >= 1:
            earlier = out_blocks[block_idx - 2] if block_idx >= 2 else None
            chip_sums[block_idx - 1], earlier, query_block = lax.optimization_barrier(
                (chip_sums[block_idx - 1], earlier, query_block)
            )
            if block_idx >= 2:
                out_blocks[block_idx - 2] = earlier
            out_blocks[block_idx - 1] = reduce_across_chips(chip_sums[block_idx - 1])
        attended = one_block(block_idx, query_block).reshape(block_rows, heads_dev * HD)
        chip_sums[block_idx] = reduce_in_chip(attended)
    own_cols, chip_sums[n_blocks - 1] = lax.optimization_barrier(
        (own_cols, chip_sums[n_blocks - 1])
    )
    out_blocks[n_blocks - 1] = reduce_across_chips(chip_sums[n_blocks - 1])
    kv_cache = write_cache(own_cols)
    layer_out = jnp.concatenate(out_blocks, axis=0)
    return (layer_out, kv_cache)


def solution(mesh):
    return jax.shard_map(
        body,
        mesh=mesh,
        in_specs=(P("seq", None), P(None, "tp"), P(), P("tp", None), P("seq"), P(), P()),
        out_specs=(P("seq", "tp"), P("seq", "tp")),
        check_vma=False,
    )
```

```python
import jax
import jax.numpy as jnp
from jax import lax
from jax.sharding import PartitionSpec as P

H = 32
KVH = 4
HD = 64
WINDOW = 2048
PAGE = 16


masked_value = -1e30


def passed_along(value, axis, steps):
    count = lax.axis_size(axis)
    leading, last = (max(0, -steps), min(count, count - steps))
    return lax.ppermute(value, axis, [(source, source + steps) for source in range(leading, last)])


def attend_band(query_block, band_block, positions_q, positions_k, starts):
    keys_block = band_block[:, :, 0, :]
    values_block = band_block[:, :, 1, :]
    head_size = query_block.shape[-1]
    scores = jnp.einsum(
        "qkgd,ckd->kgqc", query_block, keys_block, preferred_element_type=jnp.float32
    ) * head_size ** (-0.5)
    lower_bound = jnp.maximum(starts, positions_q - WINDOW + 1)
    visible = (positions_k[None, :] >= lower_bound[:, None]) & (
        positions_k[None, :] <= positions_q[:, None]
    )
    scores = jnp.where(visible, scores, masked_value)
    largest = jnp.max(scores, axis=-1, keepdims=True)
    powered = jnp.exp(scores - largest)
    row_total = jnp.sum(powered, axis=-1, keepdims=True)
    weights = powered.astype(jnp.bfloat16)
    result = (
        jnp.einsum("kgqc,ckd->kgqd", weights, values_block, preferred_element_type=jnp.float32)
        / row_total
    )
    return jnp.transpose(result, (2, 0, 1, 3)).astype(jnp.bfloat16)


def body(tokens, w_query, w_kv, w_out, seg_start, page_owner, page_slot):
    seq_index = lax.axis_index("seq")
    tp_index = lax.axis_index("tp")
    seq_count = lax.axis_size("seq")
    tp_count = lax.axis_size("tp")
    tok_rows = tokens.shape[0]
    group_size = H // KVH
    heads_dev = H // tp_count
    kv_heads_dev = max(1, heads_dev // group_size)
    kv_width = kv_heads_dev * 2 * HD
    cache_width = KVH * 2 * HD // tp_count
    first_col = tp_index * heads_dev // group_size * 2 * HD
    queries = jnp.dot(tokens, w_query, preferred_element_type=jnp.float32).astype(jnp.bfloat16)
    w_local = lax.dynamic_slice_in_dim(w_kv, first_col, kv_width, 1)
    key_value = jnp.dot(tokens, w_local, preferred_element_type=jnp.float32).astype(jnp.bfloat16)
    own_cols = lax.dynamic_slice_in_dim(
        key_value, tp_index * cache_width - first_col, cache_width, 1
    )
    def write_cache(own_cols):
        pages_dev = tok_rows // PAGE
        slots_per = max(2, 2 * pages_dev // seq_count)
        cache_slots = seq_count * slots_per
        owners_all = page_owner.reshape(seq_count, pages_dev)
        owner_hot = (
            owners_all[:, :, None] == jnp.arange(seq_count, dtype=jnp.int32)[None, None, :]
        ).astype(jnp.int32)
        local_rank = jnp.sum((jnp.cumsum(owner_hot, axis=1) - owner_hot) * owner_hot, axis=2)
        column_of = jnp.arange(seq_count, dtype=jnp.int32)[:, None] * slots_per + local_rank
        own_owner = lax.dynamic_index_in_dim(owners_all, seq_index, 0, keepdims=False)
        own_rank = lax.dynamic_index_in_dim(local_rank, seq_index, 0, keepdims=False)
        destination = own_owner * slots_per + own_rank
        send_table = (jnp.arange(cache_slots, dtype=jnp.int32)[:, None] == destination[None, :]).astype(
            jnp.bfloat16
        )
        page_rows = own_cols.reshape(pages_dev, PAGE * cache_width)
        outgoing_pages = jnp.dot(send_table, page_rows, preferred_element_type=jnp.float32).astype(
            jnp.bfloat16
        )
        outgoing_pages = outgoing_pages.reshape(seq_count, slots_per, PAGE * cache_width)
        arrived = lax.all_to_all(outgoing_pages, "seq", split_axis=0, concat_axis=0, tiled=True)
        owned_here = page_owner == seq_index
        place_table = (
            (page_slot[None, :] == jnp.arange(cache_slots, dtype=jnp.int32)[:, None])
            & owned_here[None, :]
        ).astype(jnp.bfloat16)
        pick_table = (
            column_of.reshape(-1)[:, None] == jnp.arange(cache_slots, dtype=jnp.int32)[None, :]
        ).astype(jnp.bfloat16)
        route_table = jnp.dot(place_table, pick_table, preferred_element_type=jnp.float32).astype(
            jnp.bfloat16
        )
        cache_local = jnp.dot(
            route_table,
            arrived.reshape(cache_slots, PAGE * cache_width),
            preferred_element_type=jnp.float32,
        )
        kv_cache = cache_local.astype(jnp.bfloat16).reshape(cache_slots * PAGE, cache_width)
        return kv_cache

    blocks_back = WINDOW // tok_rows
    pieces = []
    for distance in range(blocks_back, 0, -1):
        pieces.append(passed_along(key_value, "seq", distance))
    behind = jnp.concatenate(pieces, axis=0)
    band_all = jnp.concatenate([behind, key_value], axis=0).reshape(-1, kv_heads_dev, 2, HD)
    query_heads = queries.reshape(tok_rows, kv_heads_dev, heads_dev // kv_heads_dev, HD)
    block_rows = min(256, tok_rows)
    base_position = seq_index * tok_rows

    def one_block(block_idx, query_block):
        first_row = block_idx * block_rows
        band_block = lax.dynamic_slice_in_dim(band_all, first_row, WINDOW + block_rows, 0)
        starts = lax.dynamic_slice_in_dim(seg_start, first_row, block_rows, 0)
        positions_q = base_position + first_row + jnp.arange(block_rows, dtype=jnp.int32)
        positions_k = (
            base_position + first_row - WINDOW + jnp.arange(WINDOW + block_rows, dtype=jnp.int32)
        )
        return attend_band(query_block, band_block, positions_q, positions_k, starts)

    col_width = w_out.shape[1] // tp_count
    chips = tp_count // 2
    core = tp_index % 2
    chip = tp_index // 2
    swap_pairs = [(p, p ^ 1) for p in range(tp_count)]

    w_parts = w_out.reshape(w_out.shape[0], chips, 2, col_width)

    def by_shift(which):
        picked = lax.dynamic_index_in_dim(w_parts, which, 2, keepdims=False)
        doubled = jnp.concatenate([picked, picked], axis=1)
        rolled = lax.dynamic_slice_in_dim(doubled, chip, chips, 1)
        return jnp.transpose(rolled, (1, 0, 2))

    w_keep = by_shift(core)
    w_send = by_shift(1 - core)

    def reduce_in_chip(attended):
        keep = jnp.einsum("rk,jkc->jrc", attended, w_keep, preferred_element_type=jnp.float32)
        send = jnp.einsum("rk,jkc->jrc", attended, w_send, preferred_element_type=jnp.float32)
        got = lax.ppermute(send.astype(jnp.bfloat16), "tp", swap_pairs)
        keep = keep.astype(jnp.bfloat16).astype(jnp.float32)
        return (keep + got.astype(jnp.float32)).astype(jnp.bfloat16)

    def reduce_across_chips(chip_sum):
        total = chip_sum[0].astype(jnp.float32)
        for shift in range(1, chips):
            moved = lax.ppermute(
                chip_sum[shift], "tp", [(p, (p + 2 * shift) % tp_count) for p in range(tp_count)]
            )
            total = total + moved.astype(jnp.float32)
        return total.astype(jnp.bfloat16)

    n_blocks = tok_rows // block_rows
    chip_sums = [None] * n_blocks
    out_blocks = [None] * n_blocks
    for block_idx in range(n_blocks):
        query_block = query_heads[block_idx * block_rows:(block_idx + 1) * block_rows]
        if block_idx >= 1:
            earlier = out_blocks[block_idx - 2] if block_idx >= 2 else None
            chip_sums[block_idx - 1], earlier, query_block = lax.optimization_barrier(
                (chip_sums[block_idx - 1], earlier, query_block)
            )
            if block_idx >= 2:
                out_blocks[block_idx - 2] = earlier
            out_blocks[block_idx - 1] = reduce_across_chips(chip_sums[block_idx - 1])
        attended = one_block(block_idx, query_block).reshape(block_rows, heads_dev * HD)
        if block_idx == n_blocks - 1 and block_idx >= 1:
            out_blocks[block_idx - 1], attended = lax.optimization_barrier(
                (out_blocks[block_idx - 1], attended)
            )
        chip_sums[block_idx] = reduce_in_chip(attended)
    own_cols, chip_sums[n_blocks - 1] = lax.optimization_barrier(
        (own_cols, chip_sums[n_blocks - 1])
    )
    out_blocks[n_blocks - 1] = reduce_across_chips(chip_sums[n_blocks - 1])
    kv_cache = write_cache(own_cols)
    layer_out = jnp.concatenate(out_blocks, axis=0)
    return (layer_out, kv_cache)


def solution(mesh):
    return jax.shard_map(
        body,
        mesh=mesh,
        in_specs=(P("seq", None), P(None, "tp"), P(), P("tp", None), P("seq"), P(), P()),
        out_specs=(P("seq", "tp"), P("seq", "tp")),
        check_vma=False,
    )
```
